256 devices in a mesh: gx: 16 (over y, x), gy: 16 (over z, core).
Axes of the slice: x: 4, y: 4, z: 8, core: 2. Of those that a mesh axis runs over, the one named last changes fastest.
Arguments:
- energy: float32 [256, 2048, 128], P('gx', 'gy'), may hold values from 1 to 5
- coupling: float32 [256, 2048, 128], P('gx', 'gy'), may hold values from 4000 to 40000
Outputs:
- energy_next: float32 [256, 2048, 128], P('gx', 'gy')
The draws below stay inside these ranges and needn't reach their ends.
All inputs are finite; a program needn't handle non-finite values.
Results may differ from the reference program's by a relative error of at most 0.0003.
Values sent between devices are 32-bit elements; how exact they have to be, the bound alone decides.
No kernel may reach another device: no remote copies, remote signals or barrier semaphores. Data moves between devices by JAX's collectives and lax.ppermute only.
A program may use at most 64 MiB of HBM per device.

```python
import math
import jax
import jax.numpy as jnp
from jax import lax

NZ = 128
NX = 256
NY = 2048


def levels(rng, extent, shards, least, largest):
    def one(dim, blocks):
        heights = jax.random.uniform(jax.random.fold_in(jax.random.fold_in(rng, 6), dim), (blocks,), jnp.float32, least / len(shards), largest / len(shards))
        return jnp.repeat(jnp.exp(heights), extent[dim] // blocks).reshape((-1,) + (1,) * (len(extent) - dim - 1))

    gain = one(*shards[0])
    for cut in shards[1:]:
        gain = gain * one(*cut)
    return gain


def setup_inputs(seed: int = 0) -> dict:
    key_list = jax.random.split(jax.random.key(seed), 3)
    energy = jnp.clip(1.0 + 4.0 * jax.random.uniform(key_list[0], (NX, NY, NZ), jnp.float32) ** levels(key_list[0], (NX, NY, NZ), ((0, 16), (1, 16)), -0.2, 0.2), 1.0, 5.0)
    coupling = jnp.clip(jnp.exp(math.log(40000.0) - 2.3025851 * jax.random.uniform(key_list[1], (NX, NY, NZ), jnp.float32) ** levels(key_list[1], (NX, NY, NZ), ((0, 16), (1, 16)), -0.2, 0.2)), 4000.0, 40000.0)
    return {"energy": energy, "coupling": coupling}


y_weight = 0.15


def line_solve(diag_part, lower_part, upper_part, sources):
    def forward(running, row):
        prev_ratio, prev_value = running
        diag_row, lower_row, upper_row, source_row = row
        denom = diag_row - lower_row * prev_ratio
        new_ratio = upper_row / denom
        new_value = (source_row - lower_row * prev_value) / denom
        return (new_ratio, new_value), (new_ratio, new_value)

    start = (jnp.zeros(diag_part.shape[1:], jnp.float32), jnp.zeros(diag_part.shape[1:], jnp.float32))
    _, (ratios, values) = lax.scan(forward, start, (diag_part, lower_part, upper_part, sources))

    def backward(later_value, row):
        ratio_row, value_row = row
        result = value_row - ratio_row * later_value
        return result, result

    _, solved = lax.scan(backward, jnp.zeros(diag_part.shape[1:], jnp.float32), (ratios, values), reverse=True)
    return solved


def reference(energy, coupling):
    padded = jnp.pad(energy, ((0, 0), (1, 1), (0, 0)))
    source_term = energy + y_weight * (padded[:, :-2] - 2.0 * energy + padded[:, 2:])
    right_face = jnp.concatenate([coupling[1:], jnp.zeros_like(coupling[:1])], 0)
    diag_part = 1.0 + coupling + right_face
    return line_solve(diag_part, -coupling, -right_face, source_term)
```

```python
import jax
import jax.numpy as jnp
from jax import lax
from jax.sharding import PartitionSpec as P

y_weight = 0.15


def with_halo(shard, sides, width):
    for axis, dim in sides:
        size, length = (lax.axis_size(axis), shard.shape[dim])
        up = [(i, (i + 1) % size) for i in range(size - 1)]
        down = [(j, i) for i, j in up]
        last = lax.slice_in_dim(shard, length - width, length, axis=dim)
        initial = lax.slice_in_dim(shard, 0, width, axis=dim)
        before = lax.ppermute(last, axis, up)
        after = lax.ppermute(initial, axis, down)
        shard = jnp.concatenate([before, shard, after], axis=dim)
    return shard


def local_solve(coupling, source_term):
    height = coupling.shape[0]
    n = height - 1
    ratios, v_loc, v_left = [], [], []
    for r in range(n):
        diag = 1.0 + coupling[r] + coupling[r + 1]
        lower = -coupling[r]
        upper = -coupling[r + 1]
        if r == 0:
            denom = diag
            loc = source_term[0] / denom
            left = coupling[0] / denom
        else:
            denom = diag - lower * ratios[-1]
            loc = (source_term[r] - lower * v_loc[-1]) / denom
            left = (-lower * v_left[-1]) / denom
        ratios.append(upper / denom)
        v_loc.append(loc)
        v_left.append(left)
    right_last = coupling[n] / denom
    s_loc = [None] * n
    s_left = [None] * n
    s_right = [None] * n
    s_loc[n - 1] = v_loc[n - 1]
    s_left[n - 1] = v_left[n - 1]
    s_right[n - 1] = right_last
    for r in range(n - 2, -1, -1):
        s_loc[r] = v_loc[r] - ratios[r] * s_loc[r + 1]
        s_left[r] = v_left[r] - ratios[r] * s_left[r + 1]
        s_right[r] = -(ratios[r] * s_right[r + 1])
    return s_loc, s_left, s_right


def reduced_solve(lower, middle, upper, target):
    count = len(middle)
    ratios, values = [], []
    for p in range(count):
        if p == 0:
            denom = middle[0]
            value = target[0] / denom
        else:
            denom = middle[p] - lower[p] * ratios[-1]
            value = (target[p] - lower[p] * values[-1]) / denom
        ratios.append(upper[p] / denom)
        values.append(value)
    solved = [None] * count
    solved[count - 1] = values[count - 1]
    for p in range(count - 2, -1, -1):
        solved[p] = values[p] - ratios[p] * solved[p + 1]
    return solved


def body(energy, coupling):
    height, width, depth = energy.shape
    padded = with_halo(energy, (("gy", 1),), 1)
    source_term = energy + y_weight * (padded[:, :-2] - 2.0 * energy + padded[:, 2:])
    s_loc, s_left, s_right = local_solve(coupling, source_term)
    n = height - 1
    position = lax.axis_index("gx")
    own_face = coupling[height - 1]
    lower_own = jnp.where(position == 0, 0.0, -own_face * s_left[n - 1])
    middle_own = 1.0 + own_face - own_face * s_right[n - 1]
    target_own = source_term[height - 1] + own_face * s_loc[n - 1]
    face = coupling[0]
    middle_next = face - face * s_left[0]
    upper_prev = -face * s_right[0]
    target_next = face * s_loc[0]
    parts = lax.axis_size("gx")
    chunk = width // parts
    pack = jnp.stack([lower_own, middle_own, target_own, middle_next, upper_prev, target_next], 0)
    pack = pack.reshape(6, parts, chunk, depth)
    got = lax.all_to_all(pack, "gx", 1, 1, tiled=True)
    lower = [got[0, p] for p in range(parts)]
    middle = [got[1, p] + got[3, p + 1] if p + 1 < parts else got[1, p] for p in range(parts)]
    upper = [got[4, p + 1] if p + 1 < parts else jnp.zeros_like(got[4, p]) for p in range(parts)]
    target = [got[2, p] + got[5, p + 1] if p + 1 < parts else got[2, p] for p in range(parts)]
    solved = reduced_solve(lower, middle, upper, target)
    own = jnp.stack(solved, 0)
    prev = jnp.stack([jnp.zeros_like(solved[0])] + solved[:-1], 0)
    back = jnp.stack([own, prev], 0)
    back = lax.all_to_all(back, "gx", 1, 1, tiled=True)
    last_value = back[0].reshape(width, depth)
    previous = back[1].reshape(width, depth)
    rows = [s_loc[r] + s_left[r] * previous + s_right[r] * last_value for r in range(n)]
    rows.append(last_value)
    return jnp.stack(rows, 0)


def solution(mesh):
    in_specs = (P("gx", "gy", None), P("gx", "gy", None))
    out_specs = P("gx", "gy", None)
    return jax.shard_map(body, mesh=mesh, in_specs=in_specs, out_specs=out_specs, check_vma=False)
```

```python
import jax
import jax.numpy as jnp
from jax import lax
from jax.sharding import PartitionSpec as P
from jax.experimental import pallas as pl
from jax.experimental.pallas import tpu as pltpu
import os

y_weight = 0.15
tile = 8
block = 32
interpret = bool(os.environ.get("SOL_INTERPRET"))


def with_halo(shard, sides, width):
    for axis, dim in sides:
        size, length = (lax.axis_size(axis), shard.shape[dim])
        up = [(i, (i + 1) % size) for i in range(size - 1)]
        down = [(j, i) for i, j in up]
        last = lax.slice_in_dim(shard, length - width, length, axis=dim)
        initial = lax.slice_in_dim(shard, 0, width, axis=dim)
        before = lax.ppermute(last, axis, up)
        after = lax.ppermute(initial, axis, down)
        shard = jnp.concatenate([before, shard, after], axis=dim)
    return shard


def reduced_solve(lower, middle, upper, target):
    count = len(middle)
    ratios, values = [], []
    for p in range(count):
        if p == 0:
            denom = middle[0]
            value = target[0] / denom
        else:
            denom = middle[p] - lower[p] * ratios[-1]
            value = (target[p] - lower[p] * values[-1]) / denom
        ratios.append(upper[p] / denom)
        values.append(value)
    solved = [None] * count
    solved[count - 1] = values[count - 1]
    for p in range(count - 2, -1, -1):
        solved[p] = values[p] - ratios[p] * solved[p + 1]
    return solved


def forward_rows(c, s, first_extra=None, last_extra=None):
    n = len(c) - 1
    ratios, values, lefts, denom = [], [], [], None
    for r in range(n):
        diag = 1.0 + c[r] + c[r + 1]
        lower = -c[r]
        upper = -c[r + 1]
        src = s[r]
        if r == 0 and first_extra is not None:
            src = src + first_extra
        if r == n - 1 and last_extra is not None:
            src = src + last_extra
        if r == 0:
            denom = diag
            value = src / denom
            left = c[0] / denom
        else:
            denom = diag - lower * ratios[-1]
            value = (src - lower * values[-1]) / denom
            left = (-lower * lefts[-1]) / denom
        ratios.append(upper / denom)
        values.append(value)
        lefts.append(left)
    return ratios, values, lefts, denom


def pack_kernel(pos_ref, c_ref, s_ref, out_ref):
    height = c_ref.shape[0]
    n = height - 1
    first = pos_ref[0] == 0

    def step(q, carry):
        rows = pl.ds(pl.multiple_of(q * tile, tile), tile)
        c = [c_ref[r, rows, :] for r in range(height)]
        s = [s_ref[r, rows, :] for r in range(height)]
        ratios, values, lefts, denom = forward_rows(c, s)
        right = c[n] / denom
        s_loc, s_left, s_right = values[n - 1], lefts[n - 1], right
        own_face = c[n]
        lower_own = jnp.where(first, 0.0, -own_face * s_left)
        middle_own = 1.0 + own_face - own_face * s_right
        target_own = s[n] + own_face * s_loc
        for r in range(n - 2, -1, -1):
            s_loc = values[r] - ratios[r] * s_loc
            s_left = lefts[r] - ratios[r] * s_left
            s_right = -(ratios[r] * s_right)
        face = c[0]
        pieces = [lower_own, middle_own, target_own, face - face * s_left, -face * s_right, face * s_loc]
        for i, piece in enumerate(pieces):
            out_ref[q, i] = piece
        return carry

    lax.fori_loop(0, c_ref.shape[1] // tile, step, 0)


def finish_kernel(c_ref, s_ref, x_ref, out_ref):
    height = c_ref.shape[0]
    n = height - 1

    def step(q, carry):
        rows = pl.ds(pl.multiple_of(q * tile, tile), tile)
        c = [c_ref[r, rows, :] for r in range(height)]
        s = [s_ref[r, rows, :] for r in range(height)]
        last_value = x_ref[q, 0]
        previous = x_ref[q, 1]
        ratios, values, _, _ = forward_rows(c, s, c[0] * previous, c[n] * last_value)
        u = values[n - 1]
        out_ref[n - 1, rows, :] = u
        for r in range(n - 2, -1, -1):
            u = values[r] - ratios[r] * u
            out_ref[r, rows, :] = u
        out_ref[n, rows, :] = last_value
        return carry

    lax.fori_loop(0, c_ref.shape[1] // tile, step, 0)


def local_pack(position, coupling, source_term):
    height, width, depth = coupling.shape
    grid = (width // block,)
    full = pl.BlockSpec((height, block, depth), lambda g: (0, g, 0))
    per = block // tile
    return pl.pallas_call(
        pack_kernel,
        grid=grid,
        in_specs=[pl.BlockSpec(memory_space=pltpu.SMEM), full, full],
        out_specs=pl.BlockSpec((per, 6, tile, depth), lambda g: (g, 0, 0, 0)),
        out_shape=jax.ShapeDtypeStruct((width // tile, 6, tile, depth), jnp.float32),
        interpret=interpret,
    )(position, coupling, source_term)


def finish(coupling, source_term, solved):
    height, width, depth = coupling.shape
    grid = (width // block,)
    full = pl.BlockSpec((height, block, depth), lambda g: (0, g, 0))
    per = block // tile
    return pl.pallas_call(
        finish_kernel,
        grid=grid,
        in_specs=[full, full, pl.BlockSpec((per, 2, tile, depth), lambda g: (g, 0, 0, 0))],
        out_specs=full,
        out_shape=jax.ShapeDtypeStruct((height, width, depth), jnp.float32),
        interpret=interpret,
    )(coupling, source_term, solved)


def body(energy, coupling):
    height, width, depth = energy.shape
    padded = with_halo(energy, (("gy", 1),), 1)
    source_term = energy + y_weight * (padded[:, :-2] - 2.0 * energy + padded[:, 2:])
    position = lax.axis_index("gx").astype(jnp.int32).reshape(1)
    parts = lax.axis_size("gx")
    chunk = width // parts
    pack = local_pack(position, coupling, source_term)
    pack = pack.reshape(parts, chunk // tile, 6, tile, depth).transpose(2, 0, 1, 3, 4)
    pack = pack.reshape(6, parts, chunk, depth)
    got = lax.all_to_all(pack, "gx", 1, 1, tiled=True)
    lower = [got[0, p] for p in range(parts)]
    middle = [got[1, p] + got[3, p + 1] if p + 1 < parts else got[1, p] for p in range(parts)]
    upper = [got[4, p + 1] if p + 1 < parts else jnp.zeros_like(got[4, p]) for p in range(parts)]
    target = [got[2, p] + got[5, p + 1] if p + 1 < parts else got[2, p] for p in range(parts)]
    solved = reduced_solve(lower, middle, upper, target)
    own = jnp.stack(solved, 0)
    prev = jnp.stack([jnp.zeros_like(solved[0])] + solved[:-1], 0)
    back = jnp.stack([own, prev], 0)
    back = lax.all_to_all(back, "gx", 1, 1, tiled=True)
    back = back.reshape(2, width // tile, tile, depth).transpose(1, 0, 2, 3)
    return finish(coupling, source_term, back)


def solution(mesh):
    in_specs = (P("gx", "gy", None), P("gx", "gy", None))
    out_specs = P("gx", "gy", None)
    return jax.shard_map(body, mesh=mesh, in_specs=in_specs, out_specs=out_specs, check_vma=False)
```

```python
import jax
import jax.numpy as jnp
from jax import lax
from jax.sharding import PartitionSpec as P

y_weight = 0.15


def with_halo(shard, sides, width):
    for axis, dim in sides:
        size, length = (lax.axis_size(axis), shard.shape[dim])
        up = [(i, (i + 1) % size) for i in range(size - 1)]
        down = [(j, i) for i, j in up]
        last = lax.slice_in_dim(shard, length - width, length, axis=dim)
        initial = lax.slice_in_dim(shard, 0, width, axis=dim)
        before = lax.ppermute(last, axis, up)
        after = lax.ppermute(initial, axis, down)
        shard = jnp.concatenate([before, shard, after], axis=dim)
    return shard


def local_solve(coupling, source_term):
    height = coupling.shape[0]
    n = height - 1
    ratios, v_loc, v_left = [], [], []
    for r in range(n):
        diag = 1.0 + coupling[r] + coupling[r + 1]
        lower = -coupling[r]
        upper = -coupling[r + 1]
        if r == 0:
            inv = 1.0 / diag
            loc = source_term[0] * inv
            left = coupling[0] * inv
        else:
            inv = 1.0 / (diag - lower * ratios[-1])
            loc = (source_term[r] - lower * v_loc[-1]) * inv
            left = (-lower * v_left[-1]) * inv
        ratios.append(upper * inv)
        v_loc.append(loc)
        v_left.append(left)
    right_last = coupling[n] * inv
    s_loc = [None] * n
    s_left = [None] * n
    s_right = [None] * n
    s_loc[n - 1] = v_loc[n - 1]
    s_left[n - 1] = v_left[n - 1]
    s_right[n - 1] = right_last
    for r in range(n - 2, -1, -1):
        s_loc[r] = v_loc[r] - ratios[r] * s_loc[r + 1]
        s_left[r] = v_left[r] - ratios[r] * s_left[r + 1]
        s_right[r] = -(ratios[r] * s_right[r + 1])
    return s_loc, s_left, s_right


def reduced_solve(lower, middle, upper, target):
    count = len(middle)
    ratios, values = [], []
    for p in range(count):
        if p == 0:
            inv = 1.0 / middle[0]
            value = target[0] * inv
        else:
            inv = 1.0 / (middle[p] - lower[p] * ratios[-1])
            value = (target[p] - lower[p] * values[-1]) * inv
        ratios.append(upper[p] * inv)
        values.append(value)
    solved = [None] * count
    solved[count - 1] = values[count - 1]
    for p in range(count - 2, -1, -1):
        solved[p] = values[p] - ratios[p] * solved[p + 1]
    return solved


def body(energy, coupling):
    height, width, depth = energy.shape
    padded = with_halo(energy, (("gy", 1),), 1)
    source_term = energy + y_weight * (padded[:, :-2] - 2.0 * energy + padded[:, 2:])
    s_loc, s_left, s_right = local_solve(coupling, source_term)
    n = height - 1
    position = lax.axis_index("gx")
    own_face = coupling[height - 1]
    lower_own = jnp.where(position == 0, 0.0, -own_face * s_left[n - 1])
    middle_own = 1.0 + own_face - own_face * s_right[n - 1]
    target_own = source_term[height - 1] + own_face * s_loc[n - 1]
    face = coupling[0]
    middle_next = face - face * s_left[0]
    upper_prev = -face * s_right[0]
    target_next = face * s_loc[0]
    parts = lax.axis_size("gx")
    chunk = width // parts
    pack = jnp.stack([lower_own, middle_own, target_own, middle_next, upper_prev, target_next], 0)
    pack = pack.reshape(6, parts, chunk, depth)
    got = lax.all_to_all(pack, "gx", 1, 1, tiled=True)
    lower = [got[0, p] for p in range(parts)]
    middle = [got[1, p] + got[3, p + 1] if p + 1 < parts else got[1, p] for p in range(parts)]
    upper = [got[4, p + 1] if p + 1 < parts else jnp.zeros_like(got[4, p]) for p in range(parts)]
    target = [got[2, p] + got[5, p + 1] if p + 1 < parts else got[2, p] for p in range(parts)]
    solved = reduced_solve(lower, middle, upper, target)
    own = jnp.stack(solved, 0)
    prev = jnp.stack([jnp.zeros_like(solved[0])] + solved[:-1], 0)
    back = jnp.stack([own, prev], 0)
    back = lax.all_to_all(back, "gx", 1, 1, tiled=True)
    last_value = back[0].reshape(width, depth)
    previous = back[1].reshape(width, depth)
    rows = [s_loc[r] + s_left[r] * previous + s_right[r] * last_value for r in range(n)]
    rows.append(last_value)
    return jnp.stack(rows, 0)


def solution(mesh):
    in_specs = (P("gx", "gy", None), P("gx", "gy", None))
    out_specs = P("gx", "gy", None)
    return jax.shard_map(body, mesh=mesh, in_specs=in_specs, out_specs=out_specs, check_vma=False)
```

```python
import jax
import jax.numpy as jnp
from jax import lax
from jax.sharding import PartitionSpec as P

y_weight = 0.15


def with_halo(shard, sides, width):
    for axis, dim in sides:
        size, length = (lax.axis_size(axis), shard.shape[dim])
        up = [(i, (i + 1) % size) for i in range(size - 1)]
        down = [(j, i) for i, j in up]
        last = lax.slice_in_dim(shard, length - width, length, axis=dim)
        initial = lax.slice_in_dim(shard, 0, width, axis=dim)
        before = lax.ppermute(last, axis, up)
        after = lax.ppermute(initial, axis, down)
        shard = jnp.concatenate([before, shard, after], axis=dim)
    return shard


def local_solve(coupling, source_term):
    height = coupling.shape[0]
    n = height - 1
    ratios, v_loc, v_left = [], [], []
    for r in range(n):
        diag = 1.0 + coupling[r] + coupling[r + 1]
        lower = -coupling[r]
        upper = -coupling[r + 1]
        if r == 0:
            inv = 1.0 / diag
            loc = source_term[0] * inv
            left = coupling[0] * inv
        else:
            inv = 1.0 / (diag - lower * ratios[-1])
            loc = (source_term[r] - lower * v_loc[-1]) * inv
            left = (-lower * v_left[-1]) * inv
        ratios.append(upper * inv)
        v_loc.append(loc)
        v_left.append(left)
    right_last = coupling[n] * inv
    s_loc = [None] * n
    s_left = [None] * n
    s_right = [None] * n
    s_loc[n - 1] = v_loc[n - 1]
    s_left[n - 1] = v_left[n - 1]
    s_right[n - 1] = right_last
    for r in range(n - 2, -1, -1):
        s_loc[r] = v_loc[r] - ratios[r] * s_loc[r + 1]
        s_left[r] = v_left[r] - ratios[r] * s_left[r + 1]
        s_right[r] = -(ratios[r] * s_right[r + 1])
    return s_loc, s_left, s_right


def reduced_solve(lower, middle, upper, target):
    count = len(middle)
    ratios, values = [], []
    for p in range(count):
        if p == 0:
            inv = 1.0 / middle[0]
            value = target[0] * inv
        else:
            inv = 1.0 / (middle[p] - lower[p] * ratios[-1])
            value = (target[p] - lower[p] * values[-1]) * inv
        if p + 1 < count:
            ratios.append(upper[p] * inv)
        values.append(value)
    solved = [None] * count
    solved[count - 1] = values[count - 1]
    for p in range(count - 2, -1, -1):
        solved[p] = values[p] - ratios[p] * solved[p + 1]
    return solved


def body(energy, coupling):
    height, width, depth = energy.shape
    padded = with_halo(energy, (("gy", 1),), 1)
    source_term = energy + y_weight * (padded[:, :-2] - 2.0 * energy + padded[:, 2:])
    s_loc, s_left, s_right = local_solve(coupling, source_term)
    n = height - 1
    position = lax.axis_index("gx")
    own_face = coupling[height - 1]
    lower_own = jnp.where(position == 0, 0.0, -own_face * s_left[n - 1])
    middle_own = 1.0 + own_face - own_face * s_right[n - 1]
    target_own = source_term[height - 1] + own_face * s_loc[n - 1]
    face = coupling[0]
    middle_next = face - face * s_left[0]
    upper_prev = -face * s_right[0]
    target_next = face * s_loc[0]
    parts = lax.axis_size("gx")
    chunk = width // parts
    pack = jnp.stack([lower_own, middle_own, target_own, middle_next, upper_prev, target_next], 0)
    pack = pack.reshape(6, parts, chunk, depth)
    got = lax.all_to_all(pack, "gx", 1, 1, tiled=True)
    lower = [got[0, p] for p in range(parts)]
    middle = [got[1, p] + got[3, p + 1] if p + 1 < parts else got[1, p] for p in range(parts)]
    upper = [got[4, p + 1] for p in range(parts - 1)]
    target = [got[2, p] + got[5, p + 1] if p + 1 < parts else got[2, p] for p in range(parts)]
    solved = reduced_solve(lower, middle, upper, target)
    own = jnp.stack(solved, 0)
    prev = jnp.stack([solved[0] * 0.0] + solved[:-1], 0)
    back = jnp.stack([own, prev], 0)
    back = lax.all_to_all(back, "gx", 1, 1, tiled=True)
    last_value = back[0].reshape(width, depth)
    previous = back[1].reshape(width, depth)
    rows = [s_loc[r] + s_left[r] * previous + s_right[r] * last_value for r in range(n)]
    rows.append(last_value)
    return jnp.stack(rows, 0)


def solution(mesh):
    in_specs = (P("gx", "gy", None), P("gx", "gy", None))
    out_specs = P("gx", "gy", None)
    return jax.shard_map(body, mesh=mesh, in_specs=in_specs, out_specs=out_specs, check_vma=False)
```

```python
import jax
import jax.numpy as jnp
from jax import lax
from jax.sharding import PartitionSpec as P

y_weight = 0.15


def with_halo(shard, sides, width):
    for axis, dim in sides:
        size, length = (lax.axis_size(axis), shard.shape[dim])
        up = [(i, (i + 1) % size) for i in range(size - 1)]
        down = [(j, i) for i, j in up]
        last = lax.slice_in_dim(shard, length - width, length, axis=dim)
        initial = lax.slice_in_dim(shard, 0, width, axis=dim)
        before = lax.ppermute(last, axis, up)
        after = lax.ppermute(initial, axis, down)
        shard = jnp.concatenate([before, shard, after], axis=dim)
    return shard


def local_solve(coupling, source_term):
    height = coupling.shape[0]
    n = height - 1
    ratios, v_loc, v_left = [], [], []
    for r in range(n):
        diag = 1.0 + coupling[r] + coupling[r + 1]
        lower = -coupling[r]
        upper = -coupling[r + 1]
        if r == 0:
            inv = 1.0 / diag
            loc = source_term[0] * inv
            left = coupling[0] * inv
        else:
            inv = 1.0 / (diag - lower * ratios[-1])
            loc = (source_term[r] - lower * v_loc[-1]) * inv
            left = (-lower * v_left[-1]) * inv
        ratios.append(upper * inv)
        v_loc.append(loc)
        v_left.append(left)
    right_last = coupling[n] * inv
    s_loc = [None] * n
    s_left = [None] * n
    s_right = [None] * n
    s_loc[n - 1] = v_loc[n - 1]
    s_left[n - 1] = v_left[n - 1]
    s_right[n - 1] = right_last
    for r in range(n - 2, -1, -1):
        s_loc[r] = v_loc[r] - ratios[r] * s_loc[r + 1]
        s_left[r] = v_left[r] - ratios[r] * s_left[r + 1]
        s_right[r] = -(ratios[r] * s_right[r + 1])
    return s_loc, s_left, s_right


def reduced_solve(lower, middle, upper, target):
    count = len(middle)
    ratios, values = [], []
    for p in range(count):
        if p == 0:
            inv = 1.0 / middle[0]
            value = target[0] * inv
        else:
            inv = 1.0 / (middle[p] - lower[p] * ratios[-1])
            value = (target[p] - lower[p] * values[-1]) * inv
        if p + 1 < count:
            ratios.append(upper[p] * inv)
        values.append(value)
    solved = [None] * count
    solved[count - 1] = values[count - 1]
    for p in range(count - 2, -1, -1):
        solved[p] = values[p] - ratios[p] * solved[p + 1]
    return solved


def body(energy, coupling):
    height, width, depth = energy.shape
    padded = with_halo(energy, (("gy", 1),), 1)
    source_term = energy + y_weight * (padded[:, :-2] - 2.0 * energy + padded[:, 2:])
    s_loc, s_left, s_right = local_solve(coupling, source_term)
    n = height - 1
    own_face = coupling[height - 1]
    coupled = -own_face * s_left[n - 1]
    middle_own = 1.0 + own_face - own_face * s_right[n - 1]
    target_own = source_term[height - 1] + own_face * s_loc[n - 1]
    face = coupling[0]
    middle_next = face - face * s_left[0]
    target_next = face * s_loc[0]
    parts = lax.axis_size("gx")
    chunk = width // parts
    pack = jnp.stack([coupled, middle_own, target_own, middle_next, target_next], 0)
    pack = pack.reshape(5, parts, chunk, depth)
    got = lax.all_to_all(pack, "gx", 1, 1, tiled=True)
    lower = [None] + [got[0, p] for p in range(1, parts)]
    middle = [got[1, p] + got[3, p + 1] if p + 1 < parts else got[1, p] for p in range(parts)]
    upper = [got[0, p + 1] for p in range(parts - 1)]
    target = [got[2, p] + got[4, p + 1] if p + 1 < parts else got[2, p] for p in range(parts)]
    solved = reduced_solve(lower, middle, upper, target)
    own = jnp.stack(solved, 0)
    prev = jnp.stack([solved[0] * 0.0] + solved[:-1], 0)
    back = jnp.stack([own, prev], 0)
    back = lax.all_to_all(back, "gx", 1, 1, tiled=True)
    last_value = back[0].reshape(width, depth)
    previous = back[1].reshape(width, depth)
    rows = [s_loc[r] + s_left[r] * previous + s_right[r] * last_value for r in range(n)]
    rows.append(last_value)
    return jnp.stack(rows, 0)


def solution(mesh):
    in_specs = (P("gx", "gy", None), P("gx", "gy", None))
    out_specs = P("gx", "gy", None)
    return jax.shard_map(body, mesh=mesh, in_specs=in_specs, out_specs=out_specs, check_vma=False)
```

```python
import jax
import jax.numpy as jnp
from jax import lax
from jax.sharding import PartitionSpec as P

y_weight = 0.15


def with_halo(shard, sides, width):
    for axis, dim in sides:
        size, length = (lax.axis_size(axis), shard.shape[dim])
        up = [(i, (i + 1) % size) for i in range(size - 1)]
        down = [(j, i) for i, j in up]
        last = lax.slice_in_dim(shard, length - width, length, axis=dim)
        initial = lax.slice_in_dim(shard, 0, width, axis=dim)
        before = lax.ppermute(last, axis, up)
        after = lax.ppermute(initial, axis, down)
        shard = jnp.concatenate([before, shard, after], axis=dim)
    return shard


def local_solve(coupling, source_term):
    height = coupling.shape[0]
    n = height - 1
    ratios, v_loc, v_left = [], [], []
    for r in range(n):
        diag = 1.0 + coupling[r] + coupling[r + 1]
        lower = -coupling[r]
        upper = -coupling[r + 1]
        if r == 0:
            inv = 1.0 / diag
            loc = source_term[0] * inv
            left = coupling[0] * inv
        else:
            inv = 1.0 / (diag - lower * ratios[-1])
            loc = (source_term[r] - lower * v_loc[-1]) * inv
            left = (-lower * v_left[-1]) * inv
        ratios.append(upper * inv)
        v_loc.append(loc)
        v_left.append(left)
    right_last = coupling[n] * inv
    s_loc = [None] * n
    s_left = [None] * n
    s_right = [None] * n
    s_loc[n - 1] = v_loc[n - 1]
    s_left[n - 1] = v_left[n - 1]
    s_right[n - 1] = right_last
    for r in range(n - 2, -1, -1):
        s_loc[r] = v_loc[r] - ratios[r] * s_loc[r + 1]
        s_left[r] = v_left[r] - ratios[r] * s_left[r + 1]
        s_right[r] = -(ratios[r] * s_right[r + 1])
    return s_loc, s_left, s_right


def reduced_solve(lower, middle, upper, target):
    count = len(middle)
    ratios, values = [], []
    for p in range(count):
        if p == 0:
            inv = 1.0 / middle[0]
            value = target[0] * inv
        else:
            inv = 1.0 / (middle[p] - lower[p] * ratios[-1])
            value = (target[p] - lower[p] * values[-1]) * inv
        if p + 1 < count:
            ratios.append(upper[p] * inv)
        values.append(value)
    solved = [None] * count
    solved[count - 1] = values[count - 1]
    for p in range(count - 2, -1, -1):
        solved[p] = values[p] - ratios[p] * solved[p + 1]
    return solved


def body(energy, coupling):
    height, width, depth = energy.shape
    size = lax.axis_size("gy")
    up = [(i, i + 1) for i in range(size - 1)]
    down = [(i + 1, i) for i in range(size - 1)]
    before = lax.ppermute(energy[:, width - 1], "gy", up)
    after = lax.ppermute(energy[:, 0], "gy", down)
    padded = jnp.concatenate([before[:, None], energy, after[:, None]], 1)
    source_term = energy + y_weight * (padded[:, :-2] - 2.0 * energy + padded[:, 2:])
    s_loc, s_left, s_right = local_solve(coupling, source_term)
    n = height - 1
    own_face = coupling[height - 1]
    coupled = -own_face * s_left[n - 1]
    middle_own = 1.0 + own_face - own_face * s_right[n - 1]
    target_own = source_term[height - 1] + own_face * s_loc[n - 1]
    face = coupling[0]
    middle_next = face - face * s_left[0]
    target_next = face * s_loc[0]
    parts = lax.axis_size("gx")
    chunk = width // parts
    pack = jnp.stack([coupled, middle_own, target_own, middle_next, target_next], 0)
    pack = pack.reshape(5, parts, chunk, depth)
    got = lax.all_to_all(pack, "gx", 1, 1, tiled=True)
    lower = [None] + [got[0, p] for p in range(1, parts)]
    middle = [got[1, p] + got[3, p + 1] if p + 1 < parts else got[1, p] for p in range(parts)]
    upper = [got[0, p + 1] for p in range(parts - 1)]
    target = [got[2, p] + got[4, p + 1] if p + 1 < parts else got[2, p] for p in range(parts)]
    solved = reduced_solve(lower, middle, upper, target)
    own = jnp.stack(solved, 0)
    prev = jnp.stack([solved[0] * 0.0] + solved[:-1], 0)
    back = jnp.stack([own, prev], 0)
    back = lax.all_to_all(back, "gx", 1, 1, tiled=True)
    last_value = back[0].reshape(width, depth)
    previous = back[1].reshape(width, depth)
    rows = [s_loc[r] + s_left[r] * previous + s_right[r] * last_value for r in range(n)]
    rows.append(last_value)
    return jnp.stack(rows, 0)


def solution(mesh):
    in_specs = (P("gx", "gy", None), P("gx", "gy", None))
    out_specs = P("gx", "gy", None)
    return jax.shard_map(body, mesh=mesh, in_specs=in_specs, out_specs=out_specs, check_vma=False)
```
